32 devices in a mesh: parts: 2 (over y), row: 2 (over x), col: 2 (over core), layer: 4 (over z).
Axes of the slice: x: 2, y: 2, z: 4, core: 2. Of those that a mesh axis runs over, the one named last changes fastest.
Arguments:
- dosages: bfloat16 [4096, 2048], P(('layer', 'col'), ('parts', 'row')), parts along dimension 1, may hold values from -6 to 6
- expression: bfloat16 [4096, 16384], P('layer', ('col', 'row')), may hold values from -6 to 6
Outputs:
- zscores: float32 [2048, 16384], P(('parts', 'row', 'layer'), 'col'), parts along dimension 0
The draws below stay inside these ranges and needn't reach their ends.
There are 2 independent parts, one for each index of `parts`. The reference program is written for one: setup_inputs(seed, part) draws one part's arguments, and reference() takes and returns one part's arrays. A program takes and returns all parts, laid end to end along the dimension named above; an argument that names none is the same for every part. Nothing has to cross between parts.
All inputs are finite; a program needn't handle non-finite values.
Results may differ from the reference program's by a relative error of at most 0.0003.
Values may be sent and summed in bfloat16 or wider, within the bound.
No kernel may reach another device: no remote copies, remote signals or barrier semaphores. Data moves between devices by JAX's collectives and lax.ppermute only.
A program may use at most 128 MiB of HBM per device.

```python
import math
import jax
import jax.numpy as jnp

GENES = 16384
VARIANTS = 1024
SAMPLES = 4096


def level_of(rng, extent, shards, low, largest):
    level = 1.0
    for position, parts in shards:
        heights = jax.random.uniform(jax.random.fold_in(jax.random.fold_in(rng, 6), position), (parts,), jnp.float32, low / len(shards), largest / len(shards))
        level = level * jnp.repeat(jnp.exp(heights), extent[position] // parts).reshape((-1,) + (1,) * (len(extent) - 1 - position))
    return level


def scatter_about(rng, shape, scale, bound, shards=(), held_as=jnp.bfloat16):
    values = scale * jax.random.normal(rng, shape, jnp.float32)
    if shards:
        values = values * level_of(rng, shape, shards, -0.22, 0.18)
    return jnp.clip(values, -bound, bound).astype(held_as)


def setup_inputs(seed: int = 0, part: int = 0) -> dict:
    keys = jax.random.split(jax.random.key(seed), 3)
    part_keys = jax.random.split(jax.random.fold_in(keys[2], part), 3)
    return {
        "dosages": scatter_about(part_keys[0], (SAMPLES, VARIANTS), 1.0, 6.0, ((0, 8), (1, 2))),
        "expression": scatter_about(keys[1], (SAMPLES, GENES), 1.0, 6.0, ((0, 4), (1, 4))),
    }


def reference(dosages, expression):
    factor = 1.0 / math.sqrt(SAMPLES)
    cross = jnp.dot(dosages.T, expression, preferred_element_type=jnp.float32)
    return cross * factor
```

```python
import math

import jax
import jax.numpy as jnp
from jax import lax
from jax.sharding import PartitionSpec as P


def contract(left_rows, right_rows):
    return lax.dot_general(
        left_rows, right_rows, (((0,), (0,)), ((), ())), preferred_element_type=jnp.float32
    )


def full_dosages(local):
    samples = lax.all_gather(local, "col", axis=0, tiled=True)
    return lax.all_gather(samples, "row", axis=1, tiled=True)


def pick(d4, index):
    block = lax.dynamic_index_in_dim(d4, index, axis=2, keepdims=False)
    return block.reshape(block.shape[0], -1)


def on_device(dosages, expression):
    layers = lax.axis_size("layer")
    rows = lax.axis_size("row")
    layer = lax.axis_index("layer")
    row = lax.axis_index("row")
    factor = 1.0 / math.sqrt(dosages.shape[0] * lax.axis_size("col") * layers)

    samples, width = expression.shape
    block = dosages.shape[1] // layers
    half = layers // 2

    inward = [(0, 1), (layers - 1, layers - 2)]
    across = [(half - 1, half), (half, half - 1)]
    outward = [(1, 0), (layers - 2, layers - 1)]

    dosages_in = lax.ppermute(dosages, "layer", inward)
    own4 = full_dosages(dosages).reshape(samples, rows, layers, block)
    out4 = full_dosages(dosages_in).reshape(samples, rows, layers, block)

    is_left = layer < half
    outer = jnp.where(is_left, 0, layers - 1)
    near = layers - 1 - layer
    far = layers - 1 - outer

    own_far = jnp.concatenate([pick(own4, near), pick(own4, far)], axis=1)
    out_far = jnp.concatenate([pick(out4, near), pick(out4, far)], axis=1)
    own_here = pick(own4, layer)
    out_here = pick(out4, layer)
    own_outer = pick(own4, outer)
    stripe = rows * block

    chunks = max(1, min(8, width // 512))
    step = width // chunks

    output = jnp.zeros((block, rows * width), jnp.float32)
    for k in range(chunks):
        mine = expression[:, k * step:(k + 1) * step]
        theirs = lax.ppermute(mine, "layer", inward)
        sent = contract(own_far, mine) + contract(out_far, theirs)
        got = lax.ppermute(sent, "layer", across)
        to_outer = contract(own_outer, mine) + got[stripe:]
        from_inner = lax.ppermute(to_outer, "layer", outward)
        final = contract(own_here, mine) + contract(out_here, theirs) + got[:stripe] + from_inner
        final = (final * factor).reshape(rows, block, step)
        for shift in range(rows):
            target = (row + shift) % rows
            piece = lax.dynamic_index_in_dim(final, target, axis=0, keepdims=False)
            if shift:
                pairs = [(source, (source + shift) % rows) for source in range(rows)]
                piece = lax.ppermute(piece, "row", pairs)
            source = (row - shift) % rows
            output = lax.dynamic_update_slice_in_dim(output, piece, source * width + k * step, 1)
    return output


def solution(mesh):
    return jax.shard_map(
        on_device,
        mesh=mesh,
        in_specs=(P(("layer", "col"), ("parts", "row")), P("layer", ("col", "row"))),
        out_specs=P(("parts", "row", "layer"), "col"),
        check_vma=False,
    )
```

```python
import math

import jax
import jax.numpy as jnp
from jax import lax
from jax.sharding import PartitionSpec as P


def contract(left_rows, right_rows):
    return lax.dot_general(
        left_rows, right_rows, (((0,), (0,)), ((), ())), preferred_element_type=jnp.float32
    )


def gathered(value, axis, dim):
    if lax.axis_size(axis) != 2:
        return lax.all_gather(value, axis, axis=dim, tiled=True)
    other = lax.ppermute(value, axis, [(0, 1), (1, 0)])
    first = lax.axis_index(axis) == 0
    return jnp.where(
        first, jnp.concatenate([value, other], dim), jnp.concatenate([other, value], dim)
    )


def full_dosages(local):
    return gathered(gathered(local, "col", 0), "row", 1)


def pick(d4, index):
    block = lax.dynamic_index_in_dim(d4, index, axis=2, keepdims=False)
    return block.reshape(block.shape[0], -1)


def on_device(dosages, expression):
    layers = lax.axis_size("layer")
    rows = lax.axis_size("row")
    layer = lax.axis_index("layer")
    row = lax.axis_index("row")
    factor = 1.0 / math.sqrt(dosages.shape[0] * lax.axis_size("col") * layers)

    samples, width = expression.shape
    block = dosages.shape[1] // layers
    half = layers // 2

    inward = [(0, 1), (layers - 1, layers - 2)]
    across = [(half - 1, half), (half, half - 1)]
    outward = [(1, 0), (layers - 2, layers - 1)]

    dosages_in = lax.ppermute(dosages, "layer", inward)
    own4 = full_dosages(dosages).reshape(samples, rows, layers, block)
    out4 = full_dosages(dosages_in).reshape(samples, rows, layers, block)

    is_left = layer < half
    outer = jnp.where(is_left, 0, layers - 1)
    near = layers - 1 - layer
    far = layers - 1 - outer

    own_far = jnp.concatenate([pick(own4, near), pick(own4, far)], axis=1)
    out_far = jnp.concatenate([pick(out4, near), pick(out4, far)], axis=1)
    own_here = pick(own4, layer)
    out_here = pick(out4, layer)
    own_outer = pick(own4, outer)
    stripe = rows * block

    part = lax.axis_index("parts")
    chunks = 2 * max(1, min(4, width // 1024))
    step = width // chunks
    swap = [(0, 1), (1, 0)]

    def columns(k):
        return lax.dynamic_slice_in_dim(expression, k * step, step, 1)

    output = jnp.zeros((block, rows * width), jnp.float32)
    previous = None
    for j in range(chunks // 2):
        first = 2 * j + part
        second = 2 * j + 1 - part
        mine = columns(first)
        if previous is not None:
            mine, _ = lax.optimization_barrier((mine, previous))
        theirs = lax.ppermute(mine, "layer", inward)
        slot = [(first, mine, theirs), (second, columns(second), lax.ppermute(theirs, "parts", swap))]
        for k, mine, theirs in slot:
            sent = contract(own_far, mine) + contract(out_far, theirs)
            if k is first:
                previous = sent
            got = lax.ppermute(sent, "layer", across)
            to_outer = contract(own_outer, mine) + got[stripe:]
            from_inner = lax.ppermute(to_outer, "layer", outward)
            final = contract(own_here, mine) + contract(out_here, theirs) + got[:stripe] + from_inner
            final = (final * factor).reshape(rows, block, step)
            for shift in range(rows):
                target = (row + shift) % rows
                piece = lax.dynamic_index_in_dim(final, target, axis=0, keepdims=False)
                if shift:
                    pairs = [(source, (source + shift) % rows) for source in range(rows)]
                    piece = lax.ppermute(piece, "row", pairs)
                source = (row - shift) % rows
                output = lax.dynamic_update_slice_in_dim(output, piece, source * width + k * step, 1)
    return output


def solution(mesh):
    return jax.shard_map(
        on_device,
        mesh=mesh,
        in_specs=(P(("layer", "col"), ("parts", "row")), P("layer", ("col", "row"))),
        out_specs=P(("parts", "row", "layer"), "col"),
        check_vma=False,
    )
```

```python
import math

import jax
import jax.numpy as jnp
from jax import lax
from jax.sharding import PartitionSpec as P


def contract(left, right):
    return lax.dot_general(left, right, (((1,), (0,)), ((), ())), preferred_element_type=jnp.float32)


def gathered(value, axis, dim):
    if lax.axis_size(axis) != 2:
        return lax.all_gather(value, axis, axis=dim, tiled=True)
    other = lax.ppermute(value, axis, [(0, 1), (1, 0)])
    first = lax.axis_index(axis) == 0
    return jnp.where(
        first, jnp.concatenate([value, other], dim), jnp.concatenate([other, value], dim)
    )


def full_dosages(local):
    return gathered(gathered(local, "col", 1), "row", 0)


def pick(d4, index):
    block = lax.dynamic_index_in_dim(d4, index, axis=1, keepdims=False)
    return block.reshape(-1, block.shape[-1])


def on_device(dosages, expression):
    layers = lax.axis_size("layer")
    rows = lax.axis_size("row")
    layer = lax.axis_index("layer")
    row = lax.axis_index("row")
    factor = 1.0 / math.sqrt(dosages.shape[0] * lax.axis_size("col") * layers)

    samples, width = expression.shape
    block = dosages.shape[1] // layers
    half = layers // 2

    inward = [(0, 1), (layers - 1, layers - 2)]
    across = [(half - 1, half), (half, half - 1)]
    outward = [(1, 0), (layers - 2, layers - 1)]

    local = dosages.T
    local_in = lax.ppermute(local, "layer", inward)
    own4 = full_dosages(local).reshape(rows, layers, block, samples)
    out4 = full_dosages(local_in).reshape(rows, layers, block, samples)

    is_left = layer < half
    outer = jnp.where(is_left, 0, layers - 1)
    near = layers - 1 - layer
    far = layers - 1 - outer

    both_far = jnp.concatenate(
        [
            jnp.concatenate([pick(own4, near), pick(own4, far)], axis=0),
            jnp.concatenate([pick(out4, near), pick(out4, far)], axis=0),
        ],
        axis=1,
    )
    both_here = jnp.concatenate([pick(own4, layer), pick(out4, layer)], axis=1)
    own_outer = pick(own4, outer)
    stripe = rows * block

    part = lax.axis_index("parts")
    chunks = 2 * max(1, min(4, width // 1024))
    step = width // chunks
    swap = [(0, 1), (1, 0)]

    def columns(k):
        return lax.dynamic_slice_in_dim(expression, k * step, step, 1)

    output = jnp.zeros((block, rows * width), jnp.float32)
    previous = None
    for j in range(chunks // 2):
        first = 2 * j + part
        second = 2 * j + 1 - part
        mine = columns(first)
        if previous is not None:
            mine, _ = lax.optimization_barrier((mine, previous))
        theirs = lax.ppermute(mine, "layer", inward)
        slot = [(first, mine, theirs), (second, columns(second), lax.ppermute(theirs, "parts", swap))]
        for k, mine, theirs in slot:
            stacked = jnp.concatenate([mine, theirs], axis=0)
            sent = contract(both_far, stacked)
            if k is first:
                previous = sent
            got = lax.ppermute(sent, "layer", across)
            to_outer = contract(own_outer, mine) + got[stripe:]
            from_inner = lax.ppermute(to_outer, "layer", outward)
            final = contract(both_here, stacked) + got[:stripe] + from_inner
            final = (final * factor).reshape(rows, block, step)
            for shift in range(rows):
                target = (row + shift) % rows
                piece = lax.dynamic_index_in_dim(final, target, axis=0, keepdims=False)
                if shift:
                    pairs = [(source, (source + shift) % rows) for source in range(rows)]
                    piece = lax.ppermute(piece, "row", pairs)
                source = (row - shift) % rows
                output = lax.dynamic_update_slice_in_dim(output, piece, source * width + k * step, 1)
    return output


def solution(mesh):
    return jax.shard_map(
        on_device,
        mesh=mesh,
        in_specs=(P(("layer", "col"), ("parts", "row")), P("layer", ("col", "row"))),
        out_specs=P(("parts", "row", "layer"), "col"),
        check_vma=False,
    )
```

```python
import math

import jax
import jax.numpy as jnp
from jax import lax
from jax.sharding import PartitionSpec as P


def contract(left, right):
    return lax.dot_general(left, right, (((1,), (0,)), ((), ())), preferred_element_type=jnp.float32)


def gathered(value, axis, dim):
    if lax.axis_size(axis) != 2:
        return lax.all_gather(value, axis, axis=dim, tiled=True)
    other = lax.ppermute(value, axis, [(0, 1), (1, 0)])
    first = lax.axis_index(axis) == 0
    return jnp.where(
        first, jnp.concatenate([value, other], dim), jnp.concatenate([other, value], dim)
    )


def on_device(dosages, expression):
    layers = lax.axis_size("layer")
    rows = lax.axis_size("row")
    layer = lax.axis_index("layer")
    row = lax.axis_index("row")
    part = lax.axis_index("parts")
    factor = 1.0 / math.sqrt(dosages.shape[0] * lax.axis_size("col") * layers)

    samples, width = expression.shape
    block = dosages.shape[1] // layers
    half = layers // 2

    inward = [(0, 1), (layers - 1, layers - 2)]
    across = [(half - 1, half), (half, half - 1)]
    outward = [(1, 0), (layers - 2, layers - 1)]
    swap = [(0, 1), (1, 0)]

    is_left = layer < half
    outer = jnp.where(is_left, 0, layers - 1)
    near = layers - 1 - layer
    far = layers - 1 - outer

    local = dosages.T
    own = gathered(local, "col", 1).reshape(layers, block, samples)
    out = gathered(lax.ppermute(local, "layer", inward), "col", 1).reshape(layers, block, samples)

    def take(d, index):
        return lax.dynamic_index_in_dim(d, index, axis=0, keepdims=True)

    far_blocks = jnp.stack(
        [jnp.concatenate([take(own, near), take(own, far)]), jnp.concatenate([take(out, near), take(out, far)])]
    )
    far_blocks = gathered(far_blocks[None], "row", 0)
    both_far = far_blocks.transpose(2, 0, 3, 1, 4).reshape(2 * rows * block, 2 * samples)

    rest = jnp.concatenate([take(own, layer), take(out, layer), take(own, outer)])
    rest = gathered(rest[None], "row", 0)
    both_here = rest[:, :2].transpose(0, 2, 1, 3).reshape(rows * block, 2 * samples)
    own_outer = rest[:, 2].reshape(rows * block, samples)
    stripe = rows * block

    chunks = 2 * max(1, min(4, width // 1024))
    step = width // chunks

    def columns(k):
        return lax.dynamic_slice_in_dim(expression, k * step, step, 1)

    output = jnp.zeros((block, rows * width), jnp.float32)

    def finish(output, k, mine, stacked, got):
        to_outer = contract(own_outer, mine) + got[stripe:]
        from_inner = lax.ppermute(to_outer, "layer", outward)
        final = contract(both_here, stacked) + got[:stripe] + from_inner
        final = (final * factor).reshape(rows, block, step)
        for shift in range(rows):
            target = (row + shift) % rows
            piece = lax.dynamic_index_in_dim(final, target, axis=0, keepdims=False)
            if shift:
                pairs = [(source, (source + shift) % rows) for source in range(rows)]
                piece = lax.ppermute(piece, "row", pairs)
            source = (row - shift) % rows
            output = lax.dynamic_update_slice_in_dim(output, piece, source * width + k * step, 1)
        return output

    previous = None
    pending = None
    for j in range(chunks // 2):
        first = 2 * j + part
        second = 2 * j + 1 - part
        mine = columns(first)
        if previous is not None:
            mine, _ = lax.optimization_barrier((mine, previous))
        theirs = lax.ppermute(mine, "layer", inward)
        slot = [(first, mine, theirs), (second, columns(second), lax.ppermute(theirs, "parts", swap))]
        for k, mine, theirs in slot:
            stacked = jnp.concatenate([mine, theirs], axis=0)
            sent = contract(both_far, stacked)
            if k is first:
                previous = sent
            got = lax.ppermute(sent, "layer", across)
            if pending is not None:
                got_before, _ = lax.optimization_barrier((pending[3], sent))
                output = finish(output, pending[0], pending[1], pending[2], got_before)
            pending = (k, mine, stacked, got)
    output = finish(output, pending[0], pending[1], pending[2], pending[3])
    return output


def solution(mesh):
    return jax.shard_map(
        on_device,
        mesh=mesh,
        in_specs=(P(("layer", "col"), ("parts", "row")), P("layer", ("col", "row"))),
        out_specs=P(("parts", "row", "layer"), "col"),
        check_vma=False,
    )
```

```python
import math

import jax
import jax.numpy as jnp
from jax import lax
from jax.sharding import PartitionSpec as P


def contract(left, right):
    return lax.dot_general(left, right, (((1,), (0,)), ((), ())), preferred_element_type=jnp.float32)


def gathered(value, axis, dim):
    if lax.axis_size(axis) != 2:
        return lax.all_gather(value, axis, axis=dim, tiled=True)
    other = lax.ppermute(value, axis, [(0, 1), (1, 0)])
    first = lax.axis_index(axis) == 0
    return jnp.where(
        first, jnp.concatenate([value, other], dim), jnp.concatenate([other, value], dim)
    )


def on_device(dosages, expression):
    layers = lax.axis_size("layer")
    rows = lax.axis_size("row")
    layer = lax.axis_index("layer")
    row = lax.axis_index("row")
    part = lax.axis_index("parts")
    factor = 1.0 / math.sqrt(dosages.shape[0] * lax.axis_size("col") * layers)

    samples, width = expression.shape
    block = dosages.shape[1] // layers
    half = layers // 2

    inward = [(0, 1), (layers - 1, layers - 2)]
    across = [(half - 1, half), (half, half - 1)]
    outward = [(1, 0), (layers - 2, layers - 1)]
    swap = [(0, 1), (1, 0)]

    is_left = layer < half
    outer = jnp.where(is_left, 0, layers - 1)
    near = layers - 1 - layer
    far = layers - 1 - outer

    local = dosages.T
    own = gathered(local, "col", 1).reshape(layers, block, samples)
    out = gathered(lax.ppermute(local, "layer", inward), "col", 1).reshape(layers, block, samples)

    def take(d, index):
        return lax.dynamic_index_in_dim(d, index, axis=0, keepdims=True)

    far_blocks = jnp.stack(
        [jnp.concatenate([take(own, near), take(own, far)]), jnp.concatenate([take(out, near), take(out, far)])]
    )
    far_blocks = gathered(far_blocks[None], "row", 0)
    both_far = far_blocks.transpose(2, 0, 3, 1, 4).reshape(2 * rows * block, 2 * samples)

    rest = jnp.concatenate([take(own, layer), take(out, layer), take(own, outer)])
    rest = gathered(rest[None], "row", 0)
    both_here = rest[:, :2].transpose(0, 2, 1, 3).reshape(rows * block, 2 * samples)
    own_outer = rest[:, 2].reshape(rows * block, samples)
    stripe = rows * block

    chunks = 2 * max(1, min(4, width // 1024))
    step = width // chunks

    def columns(k):
        return lax.dynamic_slice_in_dim(expression, k * step, step, 1)

    output = jnp.zeros((block, rows * width), jnp.float32)

    def finish(output, k, mine, stacked, got):
        to_outer = contract(own_outer, mine) + got[stripe:]
        from_inner = lax.ppermute(to_outer, "layer", outward)
        final = contract(both_here, stacked) + got[:stripe] + from_inner
        final = (final * factor).reshape(rows, block, step)
        for shift in range(rows):
            target = (row + shift) % rows
            piece = lax.dynamic_index_in_dim(final, target, axis=0, keepdims=False)
            if shift:
                pairs = [(source, (source + shift) % rows) for source in range(rows)]
                piece = lax.ppermute(piece, "row", pairs)
            source = (row - shift) % rows
            output = lax.dynamic_update_slice_in_dim(output, piece, source * width + k * step, 1)
        return output

    previous = None
    pending = None
    for j in range(chunks // 2):
        first = 2 * j + part
        second = 2 * j + 1 - part
        mine = columns(first)
        if previous is not None:
            mine, _ = lax.optimization_barrier((mine, previous))
        theirs = lax.ppermute(mine, "layer", inward)
        slot = [(first, mine, theirs), (second, columns(second), lax.ppermute(theirs, "parts", swap))]
        for k, mine, theirs in slot:
            stacked = jnp.concatenate([mine, theirs], axis=0)
            sent = contract(both_far, stacked)
            if k is first:
                previous = stacked
            got = lax.ppermute(sent, "layer", across)
            if pending is not None:
                got_before, _ = lax.optimization_barrier((pending[3], sent))
                output = finish(output, pending[0], pending[1], pending[2], got_before)
            pending = (k, mine, stacked, got)
    output = finish(output, pending[0], pending[1], pending[2], pending[3])
    return output


def solution(mesh):
    return jax.shard_map(
        on_device,
        mesh=mesh,
        in_specs=(P(("layer", "col"), ("parts", "row")), P("layer", ("col", "row"))),
        out_specs=P(("parts", "row", "layer"), "col"),
        check_vma=False,
    )
```

```python
import math

import jax
import jax.numpy as jnp
from jax import lax
from jax.sharding import PartitionSpec as P


def contract(left, right):
    return lax.dot_general(left, right, (((1,), (0,)), ((), ())), preferred_element_type=jnp.float32)


def gathered(value, axis, dim):
    if lax.axis_size(axis) != 2:
        return lax.all_gather(value, axis, axis=dim, tiled=True)
    other = lax.ppermute(value, axis, [(0, 1), (1, 0)])
    first = lax.axis_index(axis) == 0
    return jnp.where(
        first, jnp.concatenate([value, other], dim), jnp.concatenate([other, value], dim)
    )


def on_device(dosages, expression):
    layers = lax.axis_size("layer")
    rows = lax.axis_size("row")
    layer = lax.axis_index("layer")
    row = lax.axis_index("row")
    part = lax.axis_index("parts")
    factor = 1.0 / math.sqrt(dosages.shape[0] * lax.axis_size("col") * layers)

    samples, width = expression.shape
    block = dosages.shape[1] // layers
    half = layers // 2

    inward = [(0, 1), (layers - 1, layers - 2)]
    across = [(half - 1, half), (half, half - 1)]
    outward = [(1, 0), (layers - 2, layers - 1)]
    swap = [(0, 1), (1, 0)]

    is_left = layer < half
    outer = jnp.where(is_left, 0, layers - 1)
    near = layers - 1 - layer
    far = layers - 1 - outer

    local = dosages.T
    own = gathered(local, "col", 1).reshape(layers, block, samples)
    out = gathered(lax.ppermute(local, "layer", inward), "col", 1).reshape(layers, block, samples)

    def take(d, index):
        return lax.dynamic_index_in_dim(d, index, axis=0, keepdims=True)

    far_blocks = jnp.stack(
        [jnp.concatenate([take(own, near), take(own, far)]), jnp.concatenate([take(out, near), take(out, far)])]
    )
    far_blocks = gathered(far_blocks[None], "row", 0)
    both_far = far_blocks.transpose(2, 0, 3, 1, 4).reshape(2 * rows * block, 2 * samples)

    rest = jnp.concatenate([take(own, layer), take(out, layer), take(own, outer)])
    rest = gathered(rest[None], "row", 0)
    both_here = rest[:, :2].transpose(0, 2, 1, 3).reshape(rows * block, 2 * samples)
    own_outer = rest[:, 2].reshape(rows * block, samples)
    stripe = rows * block

    chunks = 2 * max(1, min(4, width // 1024))
    step = width // chunks

    def columns(k):
        return lax.dynamic_slice_in_dim(expression, k * step, step, 1)

    output = jnp.zeros((block, rows * width), jnp.float32)

    def finish(output, k, mine, stacked, got):
        to_outer = contract(own_outer, mine) + got[stripe:]
        from_inner = lax.ppermute(to_outer, "layer", outward)
        final = contract(both_here, stacked) + got[:stripe] + from_inner
        final = (final * factor).reshape(rows, block, step)
        for shift in range(rows):
            target = (row + shift) % rows
            piece = lax.dynamic_index_in_dim(final, target, axis=0, keepdims=False)
            if shift:
                pairs = [(source, (source + shift) % rows) for source in range(rows)]
                piece = lax.ppermute(piece, "row", pairs)
            source = (row - shift) % rows
            output = lax.dynamic_update_slice_in_dim(output, piece, source * width + k * step, 1)
        return output

    previous = None
    pending = None
    for j in range(chunks // 2):
        first = 2 * j + part
        second = 2 * j + 1 - part
        mine = columns(first)
        if previous is not None:
            mine, _ = lax.optimization_barrier((mine, previous))
        theirs = lax.ppermute(mine, "layer", inward)
        swapped = lax.ppermute(theirs, "parts", swap)
        for k, mine in [(first, mine), (second, columns(second))]:
            if k is second:
                theirs = swapped
            stacked = jnp.concatenate([mine, theirs], axis=0)
            sent = contract(both_far, stacked)
            if k is first:
                previous = sent
            got = lax.ppermute(sent, "layer", across)
            if pending is not None:
                if k is first:
                    got_before, _, swapped = lax.optimization_barrier((pending[3], sent, swapped))
                else:
                    got_before, _ = lax.optimization_barrier((pending[3], sent))
                output = finish(output, pending[0], pending[1], pending[2], got_before)
            pending = (k, mine, stacked, got)
    output = finish(output, pending[0], pending[1], pending[2], pending[3])
    return output


def solution(mesh):
    return jax.shard_map(
        on_device,
        mesh=mesh,
        in_specs=(P(("layer", "col"), ("parts", "row")), P("layer", ("col", "row"))),
        out_specs=P(("parts", "row", "layer"), "col"),
        check_vma=False,
    )
```

```python
import math

import jax
import jax.numpy as jnp
from jax import lax
from jax.sharding import PartitionSpec as P


def contract(left, right):
    return lax.dot_general(left, right, (((1,), (0,)), ((), ())), preferred_element_type=jnp.float32)


def gathered(value, axis, dim):
    if lax.axis_size(axis) != 2:
        return lax.all_gather(value, axis, axis=dim, tiled=True)
    other = lax.ppermute(value, axis, [(0, 1), (1, 0)])
    first = lax.axis_index(axis) == 0
    return jnp.where(
        first, jnp.concatenate([value, other], dim), jnp.concatenate([other, value], dim)
    )


def on_device(dosages, expression):
    layers = lax.axis_size("layer")
    rows = lax.axis_size("row")
    layer = lax.axis_index("layer")
    row = lax.axis_index("row")
    part = lax.axis_index("parts")
    factor = 1.0 / math.sqrt(dosages.shape[0] * lax.axis_size("col") * layers)

    samples, width = expression.shape
    block = dosages.shape[1] // layers
    half = layers // 2

    inward = [(0, 1), (layers - 1, layers - 2)]
    across = [(half - 1, half), (half, half - 1)]
    outward = [(1, 0), (layers - 2, layers - 1)]
    swap = [(0, 1), (1, 0)]

    is_left = layer < half
    outer = jnp.where(is_left, 0, layers - 1)
    near = layers - 1 - layer
    far = layers - 1 - outer

    chunks = 2 * max(1, min(4, width // 1024))
    step = width // chunks

    def columns(k):
        return lax.dynamic_slice_in_dim(expression, k * step, step, 1)

    local = dosages.T
    own = gathered(local, "col", 1).reshape(layers, block, samples)
    opening = columns(part)
    local, opening = lax.optimization_barrier((local, opening))
    out = gathered(lax.ppermute(local, "layer", inward), "col", 1).reshape(layers, block, samples)

    def take(d, index):
        return lax.dynamic_index_in_dim(d, index, axis=0, keepdims=True)

    own_far = gathered(jnp.concatenate([take(own, near), take(own, far)])[None], "row", 0)
    out_far = gathered(jnp.concatenate([take(out, near), take(out, far)])[None], "row", 0)
    far_blocks = jnp.stack([own_far, out_far], axis=1)
    both_far = far_blocks.transpose(2, 0, 3, 1, 4).reshape(2 * rows * block, 2 * samples)

    rest = jnp.concatenate([take(own, layer), take(out, layer), take(own, outer)])
    rest = gathered(rest[None], "row", 0)
    both_here = rest[:, :2].transpose(0, 2, 1, 3).reshape(rows * block, 2 * samples)
    own_outer = rest[:, 2].reshape(rows * block, samples)
    stripe = rows * block

    output = jnp.zeros((block, rows * width), jnp.float32)

    def finish(output, k, mine, stacked, got):
        to_outer = contract(own_outer, mine) + got[stripe:]
        from_inner = lax.ppermute(to_outer, "layer", outward)
        final = contract(both_here, stacked) + got[:stripe] + from_inner
        final = (final * factor).reshape(rows, block, step)
        for shift in range(rows):
            target = (row + shift) % rows
            piece = lax.dynamic_index_in_dim(final, target, axis=0, keepdims=False)
            if shift:
                pairs = [(source, (source + shift) % rows) for source in range(rows)]
                piece = lax.ppermute(piece, "row", pairs)
            source = (row - shift) % rows
            output = lax.dynamic_update_slice_in_dim(output, piece, source * width + k * step, 1)
        return output

    previous = None
    pending = None
    for j in range(chunks // 2):
        first = 2 * j + part
        second = 2 * j + 1 - part
        mine = opening if j == 0 else columns(first)
        if previous is not None:
            mine, _ = lax.optimization_barrier((mine, previous))
        theirs = lax.ppermute(mine, "layer", inward)
        swapped = lax.ppermute(theirs, "parts", swap)
        for k, mine in [(first, mine), (second, columns(second))]:
            if k is second:
                theirs = swapped
            stacked = jnp.concatenate([mine, theirs], axis=0)
            sent = contract(both_far, stacked)
            if k is first:
                previous = sent
            got = lax.ppermute(sent, "layer", across)
            if pending is not None:
                if k is first:
                    got_before, _, swapped = lax.optimization_barrier((pending[3], sent, swapped))
                else:
                    got_before, _ = lax.optimization_barrier((pending[3], sent))
                output = finish(output, pending[0], pending[1], pending[2], got_before)
            pending = (k, mine, stacked, got)
    output = finish(output, pending[0], pending[1], pending[2], pending[3])
    return output


def solution(mesh):
    return jax.shard_map(
        on_device,
        mesh=mesh,
        in_specs=(P(("layer", "col"), ("parts", "row")), P("layer", ("col", "row"))),
        out_specs=P(("parts", "row", "layer"), "col"),
        check_vma=False,
    )
```

```python
import math

import jax
import jax.numpy as jnp
from jax import lax
from jax.sharding import PartitionSpec as P


def contract(left, right):
    return lax.dot_general(left, right, (((1,), (0,)), ((), ())), preferred_element_type=jnp.float32)


def gathered(value, axis, dim):
    if lax.axis_size(axis) != 2:
        return lax.all_gather(value, axis, axis=dim, tiled=True)
    other = lax.ppermute(value, axis, [(0, 1), (1, 0)])
    first = lax.axis_index(axis) == 0
    return jnp.where(
        first, jnp.concatenate([value, other], dim), jnp.concatenate([other, value], dim)
    )


def on_device(dosages, expression):
    layers = lax.axis_size("layer")
    rows = lax.axis_size("row")
    layer = lax.axis_index("layer")
    row = lax.axis_index("row")
    part = lax.axis_index("parts")
    factor = 1.0 / math.sqrt(dosages.shape[0] * lax.axis_size("col") * layers)

    samples, width = expression.shape
    block = dosages.shape[1] // layers
    half = layers // 2

    inward = [(0, 1), (layers - 1, layers - 2)]
    across = [(half - 1, half), (half, half - 1)]
    outward = [(1, 0), (layers - 2, layers - 1)]
    swap = [(0, 1), (1, 0)]

    is_left = layer < half
    outer = jnp.where(is_left, 0, layers - 1)
    near = layers - 1 - layer
    far = layers - 1 - outer

    if width >= 4096:
        slots = [width // 16] + [width // 8] * 3 + [width // 16]
    else:
        slots = [width // 2]
    bases = [sum(slots[:j]) * 2 for j in range(len(slots))]

    def columns(offset, size):
        return lax.dynamic_slice_in_dim(expression, offset, size, 1)

    local = dosages.T
    own = gathered(local, "col", 1).reshape(layers, block, samples)
    opening = columns(part * slots[0], slots[0])
    local, opening = lax.optimization_barrier((local, opening))
    out = gathered(lax.ppermute(local, "layer", inward), "col", 1).reshape(layers, block, samples)

    def take(d, index):
        return lax.dynamic_index_in_dim(d, index, axis=0, keepdims=True)

    own_far = gathered(jnp.concatenate([take(own, near), take(own, far)])[None], "row", 0)
    out_far = gathered(jnp.concatenate([take(out, near), take(out, far)])[None], "row", 0)
    far_blocks = jnp.stack([own_far, out_far], axis=1)
    both_far = far_blocks.transpose(2, 0, 3, 1, 4).reshape(2 * rows * block, 2 * samples)

    rest = jnp.concatenate([take(own, layer), take(out, layer), take(own, outer)])
    rest = gathered(rest[None], "row", 0)
    both_here = rest[:, :2].transpose(0, 2, 1, 3).reshape(rows * block, 2 * samples)
    own_outer = rest[:, 2].reshape(rows * block, samples)
    stripe = rows * block

    output = jnp.zeros((block, rows * width), jnp.float32)

    def finish(output, k, mine, stacked, got):
        step = mine.shape[1]
        to_outer = contract(own_outer, mine) + got[stripe:]
        from_inner = lax.ppermute(to_outer, "layer", outward)
        final = contract(both_here, stacked) + got[:stripe] + from_inner
        final = (final * factor).reshape(rows, block, step)
        for shift in range(rows):
            target = (row + shift) % rows
            piece = lax.dynamic_index_in_dim(final, target, axis=0, keepdims=False)
            if shift:
                pairs = [(source, (source + shift) % rows) for source in range(rows)]
                piece = lax.ppermute(piece, "row", pairs)
            source = (row - shift) % rows
            output = lax.dynamic_update_slice_in_dim(output, piece, source * width + k, 1)
        return output

    previous = None
    pending = None
    for j, size in enumerate(slots):
        first = bases[j] + part * size
        second = bases[j] + (1 - part) * size
        mine = opening if j == 0 else columns(first, size)
        if previous is not None:
            mine, _ = lax.optimization_barrier((mine, previous))
        theirs = lax.ppermute(mine, "layer", inward)
        swapped = lax.ppermute(theirs, "parts", swap)
        for k, mine in [(first, mine), (second, columns(second, size))]:
            if k is second:
                theirs = swapped
            stacked = jnp.concatenate([mine, theirs], axis=0)
            sent = contract(both_far, stacked)
            if k is first:
                previous = sent
            got = lax.ppermute(sent, "layer", across)
            if pending is not None:
                if k is first:
                    got_before, _, swapped = lax.optimization_barrier((pending[3], sent, swapped))
                else:
                    got_before, _ = lax.optimization_barrier((pending[3], sent))
                output = finish(output, pending[0], pending[1], pending[2], got_before)
            pending = (k, mine, stacked, got)
    output = finish(output, pending[0], pending[1], pending[2], pending[3])
    return output


def solution(mesh):
    return jax.shard_map(
        on_device,
        mesh=mesh,
        in_specs=(P(("layer", "col"), ("parts", "row")), P("layer", ("col", "row"))),
        out_specs=P(("parts", "row", "layer"), "col"),
        check_vma=False,
    )
```

```python
import math

import jax
import jax.numpy as jnp
from jax import lax
from jax.sharding import PartitionSpec as P


def contract(left, right):
    return lax.dot_general(left, right, (((1,), (0,)), ((), ())), preferred_element_type=jnp.float32)


def gathered(value, axis, dim):
    if lax.axis_size(axis) != 2:
        return lax.all_gather(value, axis, axis=dim, tiled=True)
    other = lax.ppermute(value, axis, [(0, 1), (1, 0)])
    first = lax.axis_index(axis) == 0
    return jnp.where(
        first, jnp.concatenate([value, other], dim), jnp.concatenate([other, value], dim)
    )


def on_device(dosages, expression):
    layers = lax.axis_size("layer")
    rows = lax.axis_size("row")
    layer = lax.axis_index("layer")
    row = lax.axis_index("row")
    part = lax.axis_index("parts")
    factor = 1.0 / math.sqrt(dosages.shape[0] * lax.axis_size("col") * layers)

    samples, width = expression.shape
    block = dosages.shape[1] // layers
    half = layers // 2

    inward = [(0, 1), (layers - 1, layers - 2)]
    across = [(half - 1, half), (half, half - 1)]
    outward = [(1, 0), (layers - 2, layers - 1)]
    swap = [(0, 1), (1, 0)]

    is_left = layer < half
    outer = jnp.where(is_left, 0, layers - 1)
    near = layers - 1 - layer
    far = layers - 1 - outer

    chunks = 2 * max(1, min(4, width // 1024))
    step = width // chunks

    def columns(k):
        return lax.dynamic_slice_in_dim(expression, k * step, step, 1)

    local = dosages.T
    own = gathered(local, "col", 1).reshape(layers, block, samples)
    opening = columns(part)
    local, opening = lax.optimization_barrier((local, opening))
    out = gathered(lax.ppermute(local, "layer", inward), "col", 1).reshape(layers, block, samples)

    def take(d, index):
        return lax.dynamic_index_in_dim(d, index, axis=0, keepdims=True)

    own_far = gathered(jnp.concatenate([take(own, near), take(own, far)])[None], "row", 0)
    out_far = gathered(jnp.concatenate([take(out, near), take(out, far)])[None], "row", 0)
    far_blocks = jnp.stack([own_far, out_far], axis=1)
    both_far = far_blocks.transpose(2, 0, 3, 1, 4).reshape(2 * rows * block, 2 * samples)

    rest = jnp.concatenate([take(own, layer), take(out, layer), take(own, outer)])
    rest = gathered(rest[None], "row", 0)
    both_here = rest[:, :2].transpose(0, 2, 1, 3).reshape(rows * block, 2 * samples)
    own_outer = rest[:, 2].reshape(rows * block, samples)
    stripe = rows * block

    output = jnp.zeros((block, rows * width), jnp.float32)

    def finish(output, k, mine, stacked, got):
        to_outer = contract(own_outer, mine) + got[stripe:]
        from_inner = lax.ppermute(to_outer, "layer", outward)
        final = contract(both_here, stacked) + got[:stripe] + from_inner
        final = (final * factor).reshape(rows, block, step)
        for shift in range(rows):
            target = (row + shift) % rows
            piece = lax.dynamic_index_in_dim(final, target, axis=0, keepdims=False)
            if shift:
                pairs = [(source, (source + shift) % rows) for source in range(rows)]
                piece = lax.ppermute(piece, "row", pairs)
            source = (row - shift) % rows
            output = lax.dynamic_update_slice_in_dim(output, piece, source * width + k * step, 1)
        return output

    sents = []
    pending = None
    for j in range(chunks // 2):
        first = 2 * j + part
        second = 2 * j + 1 - part
        mine = opening if j == 0 else columns(first)
        if j:
            gate = sents[0] if j == 1 else sents[2 * j - 3]
            mine, _ = lax.optimization_barrier((mine, gate))
        theirs = lax.ppermute(mine, "layer", inward)
        swapped = lax.ppermute(theirs, "parts", swap)
        for k, mine in [(first, mine), (second, columns(second))]:
            if k is second:
                theirs = swapped
            stacked = jnp.concatenate([mine, theirs], axis=0)
            sent = contract(both_far, stacked)
            sents.append(sent)
            got = lax.ppermute(sent, "layer", across)
            if pending is not None:
                if k is first:
                    got_before, _, swapped = lax.optimization_barrier((pending[3], sent, swapped))
                else:
                    got_before, _ = lax.optimization_barrier((pending[3], sent))
                output = finish(output, pending[0], pending[1], pending[2], got_before)
            pending = (k, mine, stacked, got)
    output = finish(output, pending[0], pending[1], pending[2], pending[3])
    return output


def solution(mesh):
    return jax.shard_map(
        on_device,
        mesh=mesh,
        in_specs=(P(("layer", "col"), ("parts", "row")), P("layer", ("col", "row"))),
        out_specs=P(("parts", "row", "layer"), "col"),
        check_vma=False,
    )
```

```python
import math

import jax
import jax.numpy as jnp
from jax import lax
from jax.sharding import PartitionSpec as P


def contract(left, right):
    return lax.dot_general(left, right, (((1,), (0,)), ((), ())), preferred_element_type=jnp.float32)


def gathered(value, axis, dim):
    if lax.axis_size(axis) != 2:
        return lax.all_gather(value, axis, axis=dim, tiled=True)
    other = lax.ppermute(value, axis, [(0, 1), (1, 0)])
    first = lax.axis_index(axis) == 0
    return jnp.where(
        first, jnp.concatenate([value, other], dim), jnp.concatenate([other, value], dim)
    )


def on_device(dosages, expression):
    layers = lax.axis_size("layer")
    rows = lax.axis_size("row")
    layer = lax.axis_index("layer")
    row = lax.axis_index("row")
    part = lax.axis_index("parts")
    factor = 1.0 / math.sqrt(dosages.shape[0] * lax.axis_size("col") * layers)

    samples, width = expression.shape
    block = dosages.shape[1] // layers
    half = layers // 2

    inward = [(0, 1), (layers - 1, layers - 2)]
    across = [(half - 1, half), (half, half - 1)]
    outward = [(1, 0), (layers - 2, layers - 1)]
    swap = [(0, 1), (1, 0)]

    is_left = layer < half
    outer = jnp.where(is_left, 0, layers - 1)
    near = layers - 1 - layer
    far = layers - 1 - outer

    chunks = 2 * max(1, min(4, width // 1024))
    step = width // chunks

    def columns(k):
        return lax.dynamic_slice_in_dim(expression, k * step, step, 1)

    local = dosages.T
    own = gathered(local, "col", 1).reshape(layers, block, samples)
    (early,) = lax.optimization_barrier((expression,))
    opening = jnp.where(part == 0, early[:, :step], early[:, step:2 * step])
    local, opening = lax.optimization_barrier((local, opening))
    out = gathered(lax.ppermute(local, "layer", inward), "col", 1).reshape(layers, block, samples)

    def take(d, index):
        return lax.dynamic_index_in_dim(d, index, axis=0, keepdims=True)

    own_far = gathered(jnp.concatenate([take(own, near), take(own, far)])[None], "row", 0)
    out_far = gathered(jnp.concatenate([take(out, near), take(out, far)])[None], "row", 0)
    far_blocks = jnp.stack([own_far, out_far], axis=1)
    both_far = far_blocks.transpose(2, 0, 3, 1, 4).reshape(2 * rows * block, 2 * samples)

    rest = jnp.concatenate([take(own, layer), take(out, layer), take(own, outer)])
    rest = gathered(rest[None], "row", 0)
    both_here = rest[:, :2].transpose(0, 2, 1, 3).reshape(rows * block, 2 * samples)
    own_outer = rest[:, 2].reshape(rows * block, samples)
    stripe = rows * block

    output = jnp.zeros((block, rows * width), jnp.float32)

    def finish(output, k, mine, stacked, got):
        to_outer = contract(own_outer, mine) + got[stripe:]
        from_inner = lax.ppermute(to_outer, "layer", outward)
        final = contract(both_here, stacked) + got[:stripe] + from_inner
        final = (final * factor).reshape(rows, block, step)
        for shift in range(rows):
            target = (row + shift) % rows
            piece = lax.dynamic_index_in_dim(final, target, axis=0, keepdims=False)
            if shift:
                pairs = [(source, (source + shift) % rows) for source in range(rows)]
                piece = lax.ppermute(piece, "row", pairs)
            source = (row - shift) % rows
            output = lax.dynamic_update_slice_in_dim(output, piece, source * width + k * step, 1)
        return output

    previous = None
    pending = None
    for j in range(chunks // 2):
        first = 2 * j + part
        second = 2 * j + 1 - part
        mine = opening if j == 0 else columns(first)
        if previous is not None:
            mine, _ = lax.optimization_barrier((mine, previous))
        theirs = lax.ppermute(mine, "layer", inward)
        swapped = lax.ppermute(theirs, "parts", swap)
        for k, mine in [(first, mine), (second, columns(second))]:
            if k is second:
                theirs = swapped
            stacked = jnp.concatenate([mine, theirs], axis=0)
            sent = contract(both_far, stacked)
            if k is first:
                previous = sent
            got = lax.ppermute(sent, "layer", across)
            if pending is not None:
                if k is first:
                    got_before, _, swapped = lax.optimization_barrier((pending[3], sent, swapped))
                else:
                    got_before, _ = lax.optimization_barrier((pending[3], sent))
                output = finish(output, pending[0], pending[1], pending[2], got_before)
            pending = (k, mine, stacked, got)
    output = finish(output, pending[0], pending[1], pending[2], pending[3])
    return output


def solution(mesh):
    return jax.shard_map(
        on_device,
        mesh=mesh,
        in_specs=(P(("layer", "col"), ("parts", "row")), P("layer", ("col", "row"))),
        out_specs=P(("parts", "row", "layer"), "col"),
        check_vma=False,
    )
```

```python
import math

import jax
import jax.numpy as jnp
from jax import lax
from jax.sharding import PartitionSpec as P


def contract(left, right):
    return lax.dot_general(left, right, (((1,), (0,)), ((), ())), preferred_element_type=jnp.float32)


def gathered(value, axis, dim):
    if lax.axis_size(axis) != 2:
        return lax.all_gather(value, axis, axis=dim, tiled=True)
    other = lax.ppermute(value, axis, [(0, 1), (1, 0)])
    first = lax.axis_index(axis) == 0
    return jnp.where(
        first, jnp.concatenate([value, other], dim), jnp.concatenate([other, value], dim)
    )


def on_device(dosages, expression):
    layers = lax.axis_size("layer")
    rows = lax.axis_size("row")
    layer = lax.axis_index("layer")
    row = lax.axis_index("row")
    part = lax.axis_index("parts")
    factor = 1.0 / math.sqrt(dosages.shape[0] * lax.axis_size("col") * layers)

    samples, width = expression.shape
    block = dosages.shape[1] // layers
    half = layers // 2

    inward = [(0, 1), (layers - 1, layers - 2)]
    across = [(half - 1, half), (half, half - 1)]
    outward = [(1, 0), (layers - 2, layers - 1)]
    swap = [(0, 1), (1, 0)]

    is_left = layer < half
    outer = jnp.where(is_left, 0, layers - 1)
    near = layers - 1 - layer
    far = layers - 1 - outer

    chunks = 2 * max(1, min(4, width // 1024))
    step = width // chunks

    def columns(k):
        return lax.dynamic_slice_in_dim(expression, k * step, step, 1)

    local = dosages.T
    own = gathered(local, "col", 1).reshape(layers, block, samples)
    (early,) = lax.optimization_barrier((expression,))
    opening = jnp.where(part == 0, early[:, :step], early[:, step:2 * step])
    local, opening = lax.optimization_barrier((local, opening))
    out = gathered(lax.ppermute(local, "layer", inward), "col", 1).reshape(layers, block, samples)

    def take(d, index):
        return lax.dynamic_index_in_dim(d, index, axis=0, keepdims=True)

    own_far = gathered(jnp.concatenate([take(own, near), take(own, far)])[None], "row", 0)
    out_far = gathered(jnp.concatenate([take(out, near), take(out, far)])[None], "row", 0)
    far_blocks = jnp.stack([own_far, out_far], axis=1)
    both_far = far_blocks.transpose(2, 0, 3, 1, 4).reshape(2 * rows * block, 2 * samples)

    rest = jnp.concatenate([take(own, layer), take(out, layer), take(own, outer)])
    rest = gathered(rest[None], "row", 0)
    both_here = rest[:, :2].transpose(0, 2, 1, 3).reshape(rows * block, 2 * samples)
    own_outer = rest[:, 2].reshape(rows * block, samples)
    stripe = rows * block

    output = jnp.zeros((block, rows * width), jnp.float32)

    skip = [(half, 0), (half - 1, layers - 1)]

    def finish(output, k, mine, stacked, got):
        got_here, got_far, from_inner = got
        final = contract(both_here, stacked) + got_here + got_far + from_inner
        final = (final * factor).reshape(rows, block, step)
        for shift in range(rows):
            target = (row + shift) % rows
            piece = lax.dynamic_index_in_dim(final, target, axis=0, keepdims=False)
            if shift:
                pairs = [(source, (source + shift) % rows) for source in range(rows)]
                piece = lax.ppermute(piece, "row", pairs)
            source = (row - shift) % rows
            output = lax.dynamic_update_slice_in_dim(output, piece, source * width + k * step, 1)
        return output

    previous = None
    pending = None
    for j in range(chunks // 2):
        first = 2 * j + part
        second = 2 * j + 1 - part
        mine = opening if j == 0 else columns(first)
        if previous is not None:
            mine, _ = lax.optimization_barrier((mine, previous))
        theirs = lax.ppermute(mine, "layer", inward)
        swapped = lax.ppermute(theirs, "parts", swap)
        for k, mine in [(first, mine), (second, columns(second))]:
            if k is second:
                theirs = swapped
            stacked = jnp.concatenate([mine, theirs], axis=0)
            sent = contract(both_far, stacked)
            if k is first:
                previous = sent
            got = (
                lax.ppermute(sent[:stripe], "layer", across),
                lax.ppermute(sent[stripe:], "layer", skip),
                lax.ppermute(contract(own_outer, mine), "layer", outward),
            )
            if pending is not None:
                if k is first:
                    got_before, _, swapped = lax.optimization_barrier((pending[3], sent, swapped))
                else:
                    got_before, _ = lax.optimization_barrier((pending[3], sent))
                output = finish(output, pending[0], pending[1], pending[2], got_before)
            pending = (k, mine, stacked, got)
    output = finish(output, pending[0], pending[1], pending[2], pending[3])
    return output


def solution(mesh):
    return jax.shard_map(
        on_device,
        mesh=mesh,
        in_specs=(P(("layer", "col"), ("parts", "row")), P("layer", ("col", "row"))),
        out_specs=P(("parts", "row", "layer"), "col"),
        check_vma=False,
    )
```

```python
import math

import jax
import jax.numpy as jnp
from jax import lax
from jax.sharding import PartitionSpec as P


def contract(left, right):
    return lax.dot_general(left, right, (((1,), (0,)), ((), ())), preferred_element_type=jnp.float32)


def gathered(value, axis, dim):
    if lax.axis_size(axis) != 2:
        return lax.all_gather(value, axis, axis=dim, tiled=True)
    other = lax.ppermute(value, axis, [(0, 1), (1, 0)])
    first = lax.axis_index(axis) == 0
    return jnp.where(
        first, jnp.concatenate([value, other], dim), jnp.concatenate([other, value], dim)
    )


def on_device(dosages, expression):
    layers = lax.axis_size("layer")
    rows = lax.axis_size("row")
    layer = lax.axis_index("layer")
    row = lax.axis_index("row")
    part = lax.axis_index("parts")
    factor = 1.0 / math.sqrt(dosages.shape[0] * lax.axis_size("col") * layers)

    samples, width = expression.shape
    block = dosages.shape[1] // layers
    half = layers // 2

    inward = [(0, 1), (layers - 1, layers - 2)]
    across = [(half - 1, half), (half, half - 1)]
    outward = [(1, 0), (layers - 2, layers - 1)]
    swap = [(0, 1), (1, 0)]

    is_left = layer < half
    outer = jnp.where(is_left, 0, layers - 1)
    near = layers - 1 - layer
    far = layers - 1 - outer

    chunks = 2 * max(1, min(4, width // 1024))
    step = width // chunks

    def columns(k):
        return lax.dynamic_slice_in_dim(expression, k * step, step, 1)

    local = dosages.T
    own = gathered(local, "col", 1).reshape(layers, block, samples)
    (early,) = lax.optimization_barrier((expression,))
    opening = jnp.where(part == 0, early[:, :step], early[:, step:2 * step])
    local, opening = lax.optimization_barrier((local, opening))
    out = gathered(lax.ppermute(local, "layer", inward), "col", 1).reshape(layers, block, samples)

    def take(d, index):
        return lax.dynamic_index_in_dim(d, index, axis=0, keepdims=True)

    own_far = gathered(jnp.concatenate([take(own, near), take(own, far)])[None], "row", 0)
    out_far = gathered(jnp.concatenate([take(out, near), take(out, far)])[None], "row", 0)
    far_blocks = jnp.stack([own_far, out_far], axis=1)
    both_far = far_blocks.transpose(2, 0, 3, 1, 4).reshape(2 * rows * block, 2 * samples)

    rest = jnp.concatenate([take(own, layer), take(out, layer), take(own, outer)])
    rest = gathered(rest[None], "row", 0)
    both_here = rest[:, :2].transpose(0, 2, 1, 3).reshape(rows * block, 2 * samples)
    own_outer = rest[:, 2].reshape(rows * block, samples)
    stripe = rows * block

    output = jnp.zeros((block, rows * width), jnp.float32)

    skip = [(half, 0), (half - 1, layers - 1)]

    def finish(output, k, mine, stacked, got):
        if isinstance(got, tuple):
            got_here, got_far, from_inner = got
            final = contract(both_here, stacked) + got_here + got_far + from_inner
        else:
            to_outer = contract(own_outer, mine) + got[stripe:]
            from_inner = lax.ppermute(to_outer, "layer", outward)
            final = contract(both_here, stacked) + got[:stripe] + from_inner
        final = (final * factor).reshape(rows, block, step)
        for shift in range(rows):
            target = (row + shift) % rows
            piece = lax.dynamic_index_in_dim(final, target, axis=0, keepdims=False)
            if shift:
                pairs = [(source, (source + shift) % rows) for source in range(rows)]
                piece = lax.ppermute(piece, "row", pairs)
            source = (row - shift) % rows
            output = lax.dynamic_update_slice_in_dim(output, piece, source * width + k * step, 1)
        return output

    previous = None
    pending = None
    for j in range(chunks // 2):
        first = 2 * j + part
        second = 2 * j + 1 - part
        mine = opening if j == 0 else columns(first)
        if previous is not None:
            mine, _ = lax.optimization_barrier((mine, previous))
        theirs = lax.ppermute(mine, "layer", inward)
        swapped = lax.ppermute(theirs, "parts", swap)
        for k, mine in [(first, mine), (second, columns(second))]:
            if k is second:
                theirs = swapped
            stacked = jnp.concatenate([mine, theirs], axis=0)
            sent = contract(both_far, stacked)
            if k is first:
                previous = sent
            if j == chunks // 2 - 1 and k is second:
                got = (
                    lax.ppermute(sent[:stripe], "layer", across),
                    lax.ppermute(sent[stripe:], "layer", skip),
                    lax.ppermute(contract(own_outer, mine), "layer", outward),
                )
            else:
                got = lax.ppermute(sent, "layer", across)
            if pending is not None:
                if k is first:
                    got_before, _, swapped = lax.optimization_barrier((pending[3], sent, swapped))
                else:
                    got_before, _ = lax.optimization_barrier((pending[3], sent))
                output = finish(output, pending[0], pending[1], pending[2], got_before)
            pending = (k, mine, stacked, got)
    output = finish(output, pending[0], pending[1], pending[2], pending[3])
    return output


def solution(mesh):
    return jax.shard_map(
        on_device,
        mesh=mesh,
        in_specs=(P(("layer", "col"), ("parts", "row")), P("layer", ("col", "row"))),
        out_specs=P(("parts", "row", "layer"), "col"),
        check_vma=False,
    )
```

```python
import math

import jax
import jax.numpy as jnp
from jax import lax
from jax.sharding import PartitionSpec as P


def contract(left, right):
    return lax.dot_general(left, right, (((1,), (0,)), ((), ())), preferred_element_type=jnp.float32)


def gathered(value, axis, dim):
    if lax.axis_size(axis) != 2:
        return lax.all_gather(value, axis, axis=dim, tiled=True)
    other = lax.ppermute(value, axis, [(0, 1), (1, 0)])
    first = lax.axis_index(axis) == 0
    return jnp.where(
        first, jnp.concatenate([value, other], dim), jnp.concatenate([other, value], dim)
    )


def on_device(dosages, expression):
    layers = lax.axis_size("layer")
    rows = lax.axis_size("row")
    layer = lax.axis_index("layer")
    row = lax.axis_index("row")
    part = lax.axis_index("parts")
    factor = 1.0 / math.sqrt(dosages.shape[0] * lax.axis_size("col") * layers)

    samples, width = expression.shape
    block = dosages.shape[1] // layers
    half = layers // 2

    inward = [(0, 1), (layers - 1, layers - 2)]
    across = [(half - 1, half), (half, half - 1)]
    outward = [(1, 0), (layers - 2, layers - 1)]
    swap = [(0, 1), (1, 0)]

    is_left = layer < half
    outer = jnp.where(is_left, 0, layers - 1)
    near = layers - 1 - layer
    far = layers - 1 - outer

    chunks = 2 * max(1, min(4, width // 1024))
    step = width // chunks

    def columns(k):
        return lax.dynamic_slice_in_dim(expression, k * step, step, 1)

    local = dosages.T
    own = gathered(local, "col", 1).reshape(layers, block, samples)
    (early,) = lax.optimization_barrier((expression,))
    opening = jnp.where(part == 0, early[:, :step], early[:, step:2 * step])
    local, opening = lax.optimization_barrier((local, opening))
    out = gathered(lax.ppermute(local, "layer", inward), "col", 1).reshape(layers, block, samples)

    def take(d, index):
        return lax.dynamic_index_in_dim(d, index, axis=0, keepdims=True)

    own_far = gathered(jnp.concatenate([take(own, near), take(own, far)])[None], "row", 0)
    out_far = gathered(jnp.concatenate([take(out, near), take(out, far)])[None], "row", 0)
    far_blocks = jnp.stack([own_far, out_far], axis=1)
    both_far = far_blocks.transpose(2, 0, 3, 1, 4).reshape(2 * rows * block, 2 * samples)

    rest = jnp.concatenate([take(own, layer), take(out, layer), take(own, outer)])
    rest = gathered(rest[None], "row", 0)
    both_here = rest[:, :2].transpose(0, 2, 1, 3).reshape(rows * block, 2 * samples)
    own_outer = rest[:, 2].reshape(rows * block, samples)
    stripe = rows * block

    output = jnp.zeros((block, rows * width), jnp.float32)

    skip = [(half, 0), (half - 1, layers - 1)]

    def finish(output, k, mine, stacked, got):
        if isinstance(got, tuple):
            got_here, got_far, from_inner = got
            final = contract(both_here, stacked) + got_here + got_far + from_inner
        else:
            to_outer = contract(own_outer, mine) + got[stripe:]
            from_inner = lax.ppermute(to_outer, "layer", outward)
            final = contract(both_here, stacked) + got[:stripe] + from_inner
        final = (final * factor).reshape(rows, block, step)
        for shift in range(rows):
            target = (row + shift) % rows
            piece = lax.dynamic_index_in_dim(final, target, axis=0, keepdims=False)
            if shift:
                pairs = [(source, (source + shift) % rows) for source in range(rows)]
                piece = lax.ppermute(piece, "row", pairs)
            source = (row - shift) % rows
            output = lax.dynamic_update_slice_in_dim(output, piece, source * width + k * step, 1)
        return output

    previous = None
    pending = None
    for j in range(chunks // 2):
        first = 2 * j + part
        second = 2 * j + 1 - part
        mine = opening if j == 0 else columns(first)
        if previous is not None:
            mine, _ = lax.optimization_barrier((mine, previous))
        theirs = lax.ppermute(mine, "layer", inward)
        swapped = lax.ppermute(theirs, "parts", swap)
        for k, mine in [(first, mine), (second, columns(second))]:
            if k is second:
                theirs = swapped
            stacked = jnp.concatenate([mine, theirs], axis=0)
            sent = contract(both_far, stacked)
            if k is first:
                previous = sent
            if j == chunks // 2 - 1:
                got = (
                    lax.ppermute(sent[:stripe], "layer", across),
                    lax.ppermute(sent[stripe:], "layer", skip),
                    lax.ppermute(contract(own_outer, mine), "layer", outward),
                )
            else:
                got = lax.ppermute(sent, "layer", across)
            if pending is not None:
                if k is first:
                    got_before, _, swapped = lax.optimization_barrier((pending[3], sent, swapped))
                else:
                    got_before, _ = lax.optimization_barrier((pending[3], sent))
                output = finish(output, pending[0], pending[1], pending[2], got_before)
            pending = (k, mine, stacked, got)
    output = finish(output, pending[0], pending[1], pending[2], pending[3])
    return output


def solution(mesh):
    return jax.shard_map(
        on_device,
        mesh=mesh,
        in_specs=(P(("layer", "col"), ("parts", "row")), P("layer", ("col", "row"))),
        out_specs=P(("parts", "row", "layer"), "col"),
        check_vma=False,
    )
```

```python
import math

import jax
import jax.numpy as jnp
from jax import lax
from jax.sharding import PartitionSpec as P


def contract(left, right):
    return lax.dot_general(left, right, (((1,), (0,)), ((), ())), preferred_element_type=jnp.float32)


def gathered(value, axis, dim):
    if lax.axis_size(axis) != 2:
        return lax.all_gather(value, axis, axis=dim, tiled=True)
    other = lax.ppermute(value, axis, [(0, 1), (1, 0)])
    first = lax.axis_index(axis) == 0
    return jnp.where(
        first, jnp.concatenate([value, other], dim), jnp.concatenate([other, value], dim)
    )


def on_device(dosages, expression):
    layers = lax.axis_size("layer")
    rows = lax.axis_size("row")
    layer = lax.axis_index("layer")
    row = lax.axis_index("row")
    part = lax.axis_index("parts")
    factor = 1.0 / math.sqrt(dosages.shape[0] * lax.axis_size("col") * layers)

    samples, width = expression.shape
    block = dosages.shape[1] // layers
    half = layers // 2

    inward = [(0, 1), (layers - 1, layers - 2)]
    across = [(half - 1, half), (half, half - 1)]
    outward = [(1, 0), (layers - 2, layers - 1)]
    swap = [(0, 1), (1, 0)]

    is_left = layer < half
    outer = jnp.where(is_left, 0, layers - 1)
    near = layers - 1 - layer
    far = layers - 1 - outer

    chunks = 2 * max(1, min(4, width // 1024))
    step = width // chunks

    def columns(k):
        return lax.dynamic_slice_in_dim(expression, k * step, step, 1)

    local = dosages.T
    own = gathered(local, "col", 1).reshape(layers, block, samples)
    (early,) = lax.optimization_barrier((expression,))
    opening = jnp.where(part == 0, early[:, :step], early[:, step:2 * step])
    local, opening = lax.optimization_barrier((local, opening))
    out = gathered(lax.ppermute(local, "layer", inward), "col", 1).reshape(layers, block, samples)

    def take(d, index):
        return lax.dynamic_index_in_dim(d, index, axis=0, keepdims=True)

    own_far = gathered(jnp.concatenate([take(own, near), take(own, far)])[None], "row", 0)
    out_far = gathered(jnp.concatenate([take(out, near), take(out, far)])[None], "row", 0)
    far_blocks = jnp.stack([own_far, out_far], axis=1)
    both_far = far_blocks.transpose(2, 0, 3, 1, 4).reshape(2 * rows * block, 2 * samples)

    rest = jnp.concatenate([take(own, layer), take(out, layer), take(own, outer)])
    rest = gathered(rest[None], "row", 0)
    both_here = rest[:, :2].transpose(0, 2, 1, 3).reshape(rows * block, 2 * samples)
    own_outer = rest[:, 2].reshape(rows * block, samples)
    stripe = rows * block

    output = jnp.zeros((block, rows * width), jnp.float32)

    skip = [(half, 0), (half - 1, layers - 1)]

    def finish(output, k, mine, stacked, got):
        if isinstance(got, tuple):
            got_here, got_far, from_inner = got
            final = contract(both_here, stacked) + got_here + got_far + from_inner
        else:
            to_outer = contract(own_outer, mine) + got[stripe:]
            from_inner = lax.ppermute(to_outer, "layer", outward)
            final = contract(both_here, stacked) + got[:stripe] + from_inner
        final = (final * factor).reshape(rows, block, step)
        for shift in range(rows):
            target = (row + shift) % rows
            piece = lax.dynamic_index_in_dim(final, target, axis=0, keepdims=False)
            if shift:
                pairs = [(source, (source + shift) % rows) for source in range(rows)]
                piece = lax.ppermute(piece, "row", pairs)
            source = (row - shift) % rows
            output = lax.dynamic_update_slice_in_dim(output, piece, source * width + k * step, 1)
        return output

    previous = None
    pending = None
    for j in range(chunks // 2):
        first = 2 * j + part
        second = 2 * j + 1 - part
        mine = opening if j == 0 else columns(first)
        if previous is not None:
            mine, _ = lax.optimization_barrier((mine, previous))
        theirs = lax.ppermute(mine, "layer", inward)
        swapped = lax.ppermute(theirs, "parts", swap)
        for k, mine in [(first, mine), (second, columns(second))]:
            if k is second:
                theirs = swapped
            stacked = jnp.concatenate([mine, theirs], axis=0)
            sent = contract(both_far, stacked)
            if k is first:
                previous = sent
            if j >= chunks // 2 - 2:
                got = (
                    lax.ppermute(sent[:stripe], "layer", across),
                    lax.ppermute(sent[stripe:], "layer", skip),
                    lax.ppermute(contract(own_outer, mine), "layer", outward),
                )
            else:
                got = lax.ppermute(sent, "layer", across)
            if pending is not None:
                if k is first:
                    got_before, _, swapped = lax.optimization_barrier((pending[3], sent, swapped))
                else:
                    got_before, _ = lax.optimization_barrier((pending[3], sent))
                output = finish(output, pending[0], pending[1], pending[2], got_before)
            pending = (k, mine, stacked, got)
    output = finish(output, pending[0], pending[1], pending[2], pending[3])
    return output


def solution(mesh):
    return jax.shard_map(
        on_device,
        mesh=mesh,
        in_specs=(P(("layer", "col"), ("parts", "row")), P("layer", ("col", "row"))),
        out_specs=P(("parts", "row", "layer"), "col"),
        check_vma=False,
    )
```

```python
import math

import jax
import jax.numpy as jnp
from jax import lax
from jax.sharding import PartitionSpec as P


def contract(left, right):
    return lax.dot_general(left, right, (((1,), (0,)), ((), ())), preferred_element_type=jnp.float32)


def gathered(value, axis, dim):
    if lax.axis_size(axis) != 2:
        return lax.all_gather(value, axis, axis=dim, tiled=True)
    other = lax.ppermute(value, axis, [(0, 1), (1, 0)])
    first = lax.axis_index(axis) == 0
    return jnp.where(
        first, jnp.concatenate([value, other], dim), jnp.concatenate([other, value], dim)
    )


def on_device(dosages, expression):
    layers = lax.axis_size("layer")
    rows = lax.axis_size("row")
    layer = lax.axis_index("layer")
    row = lax.axis_index("row")
    part = lax.axis_index("parts")
    factor = 1.0 / math.sqrt(dosages.shape[0] * lax.axis_size("col") * layers)

    samples, width = expression.shape
    block = dosages.shape[1] // layers
    half = layers // 2

    inward = [(0, 1), (layers - 1, layers - 2)]
    across = [(half - 1, half), (half, half - 1)]
    outward = [(1, 0), (layers - 2, layers - 1)]
    swap = [(0, 1), (1, 0)]

    is_left = layer < half
    outer = jnp.where(is_left, 0, layers - 1)
    near = layers - 1 - layer
    far = layers - 1 - outer

    chunks = 2 * max(1, min(4, width // 1024))
    step = width // chunks

    def columns(k):
        return lax.dynamic_slice_in_dim(expression, k * step, step, 1)

    local = dosages.T
    own = gathered(local, "col", 1).reshape(layers, block, samples)
    (early,) = lax.optimization_barrier((expression,))
    opening = jnp.where(part == 0, early[:, :step], early[:, step:2 * step])
    local, opening = lax.optimization_barrier((local, opening))
    out = gathered(lax.ppermute(local, "layer", inward), "col", 1).reshape(layers, block, samples)

    def take(d, index):
        return lax.dynamic_index_in_dim(d, index, axis=0, keepdims=True)

    own_far = gathered(jnp.concatenate([take(own, near), take(own, far)])[None], "row", 0)
    out_far = gathered(jnp.concatenate([take(out, near), take(out, far)])[None], "row", 0)
    far_blocks = jnp.stack([own_far, out_far], axis=1)
    both_far = far_blocks.transpose(2, 0, 3, 1, 4).reshape(2 * rows * block, 2 * samples)

    rest = jnp.concatenate([take(own, layer), take(out, layer), take(own, outer)])
    rest = gathered(rest[None], "row", 0)
    both_here = rest[:, :2].transpose(0, 2, 1, 3).reshape(rows * block, 2 * samples)
    own_outer = rest[:, 2].reshape(rows * block, samples)
    stripe = rows * block

    output = jnp.zeros((block, rows * width), jnp.float32)

    skip = [(half, 0), (half - 1, layers - 1)]

    def finish(output, k, mine, stacked, got):
        if isinstance(got, tuple):
            got_here, got_far, from_inner = got
            final = contract(both_here, stacked) + got_here + got_far + from_inner
        else:
            to_outer = contract(own_outer, mine) + got[stripe:]
            from_inner = lax.ppermute(to_outer, "layer", outward)
            final = contract(both_here, stacked) + got[:stripe] + from_inner
        final = (final * factor).reshape(rows, block, step)
        for shift in range(rows):
            target = (row + shift) % rows
            piece = lax.dynamic_index_in_dim(final, target, axis=0, keepdims=False)
            if shift:
                pairs = [(source, (source + shift) % rows) for source in range(rows)]
                piece = lax.ppermute(piece, "row", pairs)
            source = (row - shift) % rows
            output = lax.dynamic_update_slice_in_dim(output, piece, source * width + k * step, 1)
        return output

    previous = None
    pending = None
    for j in range(chunks // 2):
        first = 2 * j + part
        second = 2 * j + 1 - part
        mine = opening if j == 0 else columns(first)
        if previous is not None:
            mine, _ = lax.optimization_barrier((mine, previous))
        theirs = lax.ppermute(mine, "layer", inward)
        swapped = lax.ppermute(theirs, "parts", swap)
        for k, mine in [(first, mine), (second, columns(second))]:
            if k is second:
                theirs = swapped
            stacked = jnp.concatenate([mine, theirs], axis=0)
            sent = contract(both_far, stacked)
            if k is first:
                previous = sent
            if j == chunks // 2 - 1 or (j == chunks // 2 - 2 and k is second):
                got = (
                    lax.ppermute(sent[:stripe], "layer", across),
                    lax.ppermute(sent[stripe:], "layer", skip),
                    lax.ppermute(contract(own_outer, mine), "layer", outward),
                )
            else:
                got = lax.ppermute(sent, "layer", across)
            if pending is not None:
                if k is first:
                    got_before, _, swapped = lax.optimization_barrier((pending[3], sent, swapped))
                else:
                    got_before, _ = lax.optimization_barrier((pending[3], sent))
                output = finish(output, pending[0], pending[1], pending[2], got_before)
            pending = (k, mine, stacked, got)
    output = finish(output, pending[0], pending[1], pending[2], pending[3])
    return output


def solution(mesh):
    return jax.shard_map(
        on_device,
        mesh=mesh,
        in_specs=(P(("layer", "col"), ("parts", "row")), P("layer", ("col", "row"))),
        out_specs=P(("parts", "row", "layer"), "col"),
        check_vma=False,
    )
```

```python
import math

import jax
import jax.numpy as jnp
from jax import lax
from jax.sharding import PartitionSpec as P


def contract(left, right):
    return lax.dot_general(left, right, (((1,), (0,)), ((), ())), preferred_element_type=jnp.float32)


def gathered(value, axis, dim):
    if lax.axis_size(axis) != 2:
        return lax.all_gather(value, axis, axis=dim, tiled=True)
    other = lax.ppermute(value, axis, [(0, 1), (1, 0)])
    first = lax.axis_index(axis) == 0
    return jnp.where(
        first, jnp.concatenate([value, other], dim), jnp.concatenate([other, value], dim)
    )


def on_device(dosages, expression):
    layers = lax.axis_size("layer")
    rows = lax.axis_size("row")
    layer = lax.axis_index("layer")
    row = lax.axis_index("row")
    part = lax.axis_index("parts")
    factor = 1.0 / math.sqrt(dosages.shape[0] * lax.axis_size("col") * layers)

    samples, width = expression.shape
    block = dosages.shape[1] // layers
    half = layers // 2

    inward = [(0, 1), (layers - 1, layers - 2)]
    across = [(half - 1, half), (half, half - 1)]
    outward = [(1, 0), (layers - 2, layers - 1)]
    swap = [(0, 1), (1, 0)]

    is_left = layer < half
    outer = jnp.where(is_left, 0, layers - 1)
    near = layers - 1 - layer
    far = layers - 1 - outer

    chunks = 2 * max(1, min(4, width // 1024))
    step = width // chunks

    def columns(k):
        return lax.dynamic_slice_in_dim(expression, k * step, step, 1)

    local = dosages.T
    own = gathered(local, "col", 1).reshape(layers, block, samples)
    (early,) = lax.optimization_barrier((expression,))
    opening = jnp.where(part == 0, early[:, :step], early[:, step:2 * step])
    local, opening = lax.optimization_barrier((local, opening))
    others = jnp.stack(
        [
            lax.dynamic_index_in_dim(local.reshape(layers, block, -1), (layer + 1 + i) % layers, 0, False)
            for i in range(layers - 1)
        ]
    )
    out = gathered(lax.ppermute(others, "layer", inward), "col", 2)

    def take(d, index):
        return lax.dynamic_index_in_dim(d, index, axis=0, keepdims=True)

    def take_out(index):
        return take(out, (index - outer - 1) % layers)

    own_far = gathered(jnp.concatenate([take(own, near), take(own, far)])[None], "row", 0)
    out_far = gathered(jnp.concatenate([take_out(near), take_out(far)])[None], "row", 0)
    far_blocks = jnp.stack([own_far, out_far], axis=1)
    both_far = far_blocks.transpose(2, 0, 3, 1, 4).reshape(2 * rows * block, 2 * samples)

    rest = jnp.concatenate([take(own, layer), take_out(layer), take(own, outer)])
    rest = gathered(rest[None], "row", 0)
    both_here = rest[:, :2].transpose(0, 2, 1, 3).reshape(rows * block, 2 * samples)
    own_outer = rest[:, 2].reshape(rows * block, samples)
    stripe = rows * block

    output = jnp.zeros((block, rows * width), jnp.float32)

    skip = [(half, 0), (half - 1, layers - 1)]

    def finish(output, k, mine, stacked, got):
        if isinstance(got, tuple):
            got_here, got_far, from_inner = got
            final = contract(both_here, stacked) + got_here + got_far + from_inner
        else:
            to_outer = contract(own_outer, mine) + got[stripe:]
            from_inner = lax.ppermute(to_outer, "layer", outward)
            final = contract(both_here, stacked) + got[:stripe] + from_inner
        final = (final * factor).reshape(rows, block, step)
        for shift in range(rows):
            target = (row + shift) % rows
            piece = lax.dynamic_index_in_dim(final, target, axis=0, keepdims=False)
            if shift:
                pairs = [(source, (source + shift) % rows) for source in range(rows)]
                piece = lax.ppermute(piece, "row", pairs)
            source = (row - shift) % rows
            output = lax.dynamic_update_slice_in_dim(output, piece, source * width + k * step, 1)
        return output

    previous = None
    pending = None
    for j in range(chunks // 2):
        first = 2 * j + part
        second = 2 * j + 1 - part
        mine = opening if j == 0 else columns(first)
        if previous is not None:
            mine, _ = lax.optimization_barrier((mine, previous))
        theirs = lax.ppermute(mine, "layer", inward)
        swapped = lax.ppermute(theirs, "parts", swap)
        for k, mine in [(first, mine), (second, columns(second))]:
            if k is second:
                theirs = swapped
            stacked = jnp.concatenate([mine, theirs], axis=0)
            sent = contract(both_far, stacked)
            if k is first:
                previous = sent
            if j == chunks // 2 - 1:
                got = (
                    lax.ppermute(sent[:stripe], "layer", across),
                    lax.ppermute(sent[stripe:], "layer", skip),
                    lax.ppermute(contract(own_outer, mine), "layer", outward),
                )
            else:
                got = lax.ppermute(sent, "layer", across)
            if pending is not None:
                if k is first:
                    got_before, _, swapped = lax.optimization_barrier((pending[3], sent, swapped))
                else:
                    got_before, _ = lax.optimization_barrier((pending[3], sent))
                output = finish(output, pending[0], pending[1], pending[2], got_before)
            pending = (k, mine, stacked, got)
    output = finish(output, pending[0], pending[1], pending[2], pending[3])
    return output


def solution(mesh):
    return jax.shard_map(
        on_device,
        mesh=mesh,
        in_specs=(P(("layer", "col"), ("parts", "row")), P("layer", ("col", "row"))),
        out_specs=P(("parts", "row", "layer"), "col"),
        check_vma=False,
    )
```

```python
import math

import jax
import jax.numpy as jnp
from jax import lax
from jax.sharding import PartitionSpec as P


def contract(left, right):
    return lax.dot_general(left, right, (((1,), (0,)), ((), ())), preferred_element_type=jnp.float32)


def gathered(value, axis, dim):
    if lax.axis_size(axis) != 2:
        return lax.all_gather(value, axis, axis=dim, tiled=True)
    other = lax.ppermute(value, axis, [(0, 1), (1, 0)])
    first = lax.axis_index(axis) == 0
    return jnp.where(
        first, jnp.concatenate([value, other], dim), jnp.concatenate([other, value], dim)
    )


def on_device(dosages, expression):
    layers = lax.axis_size("layer")
    rows = lax.axis_size("row")
    layer = lax.axis_index("layer")
    row = lax.axis_index("row")
    part = lax.axis_index("parts")
    factor = 1.0 / math.sqrt(dosages.shape[0] * lax.axis_size("col") * layers)

    samples, width = expression.shape
    block = dosages.shape[1] // layers
    half = layers // 2

    inward = [(0, 1), (layers - 1, layers - 2)]
    across = [(half - 1, half), (half, half - 1)]
    outward = [(1, 0), (layers - 2, layers - 1)]
    swap = [(0, 1), (1, 0)]

    is_left = layer < half
    outer = jnp.where(is_left, 0, layers - 1)
    near = layers - 1 - layer
    far = layers - 1 - outer

    chunks = 2 * max(1, min(4, width // 1024))
    step = width // chunks

    def columns(k):
        return lax.dynamic_slice_in_dim(expression, k * step, step, 1)

    local = dosages.T
    own = gathered(local, "col", 1).reshape(layers, block, samples)
    (early,) = lax.optimization_barrier((expression,))
    opening = jnp.where(part == 0, early[:, :step], early[:, step:2 * step])
    local, opening = lax.optimization_barrier((local, opening))
    others = jnp.stack(
        [
            lax.dynamic_index_in_dim(local.reshape(layers, block, -1), (layer + 1 + i) % layers, 0, False)
            for i in range(layers - 1)
        ]
    )
    out = gathered(lax.ppermute(others, "layer", inward), "col", 2)

    def take(d, index):
        return lax.dynamic_index_in_dim(d, index, axis=0, keepdims=True)

    def take_out(index):
        return take(out, (index - outer - 1) % layers)

    own_far = gathered(jnp.concatenate([take(own, near), take(own, far)])[None], "row", 0)
    out_far = gathered(jnp.concatenate([take_out(near), take_out(far)])[None], "row", 0)
    far_blocks = jnp.stack([own_far, out_far], axis=1)
    both_far = far_blocks.transpose(2, 0, 3, 1, 4).reshape(2 * rows * block, 2 * samples)

    rest = jnp.concatenate([take(own, layer), take_out(layer), take(own, outer)])
    rest = gathered(rest[None], "row", 0)
    both_here = rest[:, :2].transpose(0, 2, 1, 3).reshape(rows * block, 2 * samples)
    own_outer = rest[:, 2].reshape(rows * block, samples)
    stripe = rows * block

    output = jnp.zeros((block, rows * width), jnp.float32)

    skip = [(half, 0), (half - 1, layers - 1)]

    def finish(output, k, mine, stacked, got):
        if isinstance(got, tuple):
            got_here, got_far, from_inner = got
            final = contract(both_here, stacked) + got_here + got_far + from_inner
        else:
            to_outer = contract(own_outer, mine) + got[stripe:]
            from_inner = lax.ppermute(to_outer, "layer", outward)
            final = contract(both_here, stacked) + got[:stripe] + from_inner
        final = (final * factor).reshape(rows, block, step)
        for shift in range(rows):
            target = (row + shift) % rows
            piece = lax.dynamic_index_in_dim(final, target, axis=0, keepdims=False)
            if shift:
                pairs = [(source, (source + shift) % rows) for source in range(rows)]
                piece = lax.ppermute(piece, "row", pairs)
            source = (row - shift) % rows
            output = lax.dynamic_update_slice_in_dim(output, piece, source * width + k * step, 1)
        return output

    previous = None
    pending = None
    for j in range(chunks // 2):
        first = 2 * j + part
        second = 2 * j + 1 - part
        mine = opening if j == 0 else columns(first)
        if previous is not None:
            mine, _ = lax.optimization_barrier((mine, previous))
        theirs = lax.ppermute(mine, "layer", inward)
        swapped = lax.ppermute(theirs, "parts", swap)
        for k, mine in [(first, mine), (second, columns(second))]:
            if k is second:
                theirs = swapped
            stacked = jnp.concatenate([mine, theirs], axis=0)
            sent = contract(both_far, stacked)
            if k is first:
                previous = sent if j == 0 else stacked
            if j == chunks // 2 - 1:
                got = (
                    lax.ppermute(sent[:stripe], "layer", across),
                    lax.ppermute(sent[stripe:], "layer", skip),
                    lax.ppermute(contract(own_outer, mine), "layer", outward),
                )
            else:
                got = lax.ppermute(sent, "layer", across)
            if pending is not None:
                if k is first:
                    got_before, _, swapped = lax.optimization_barrier((pending[3], sent, swapped))
                else:
                    got_before, _ = lax.optimization_barrier((pending[3], sent))
                output = finish(output, pending[0], pending[1], pending[2], got_before)
            pending = (k, mine, stacked, got)
    output = finish(output, pending[0], pending[1], pending[2], pending[3])
    return output


def solution(mesh):
    return jax.shard_map(
        on_device,
        mesh=mesh,
        in_specs=(P(("layer", "col"), ("parts", "row")), P("layer", ("col", "row"))),
        out_specs=P(("parts", "row", "layer"), "col"),
        check_vma=False,
    )
```

```python
import math

import jax
import jax.numpy as jnp
from jax import lax
from jax.sharding import PartitionSpec as P


def contract(left, right):
    return lax.dot_general(left, right, (((1,), (0,)), ((), ())), preferred_element_type=jnp.float32)


def gathered(value, axis, dim):
    if lax.axis_size(axis) != 2:
        return lax.all_gather(value, axis, axis=dim, tiled=True)
    other = lax.ppermute(value, axis, [(0, 1), (1, 0)])
    first = lax.axis_index(axis) == 0
    return jnp.where(
        first, jnp.concatenate([value, other], dim), jnp.concatenate([other, value], dim)
    )


def on_device(dosages, expression):
    layers = lax.axis_size("layer")
    rows = lax.axis_size("row")
    layer = lax.axis_index("layer")
    row = lax.axis_index("row")
    part = lax.axis_index("parts")
    factor = 1.0 / math.sqrt(dosages.shape[0] * lax.axis_size("col") * layers)

    samples, width = expression.shape
    block = dosages.shape[1] // layers
    half = layers // 2

    inward = [(0, 1), (layers - 1, layers - 2)]
    across = [(half - 1, half), (half, half - 1)]
    outward = [(1, 0), (layers - 2, layers - 1)]
    swap = [(0, 1), (1, 0)]

    is_left = layer < half
    outer = jnp.where(is_left, 0, layers - 1)
    near = layers - 1 - layer
    far = layers - 1 - outer

    chunks = 2 * max(1, min(4, width // 1024))
    step = width // chunks

    def columns(k):
        return lax.dynamic_slice_in_dim(expression, k * step, step, 1)

    local = dosages.T
    own = gathered(local, "col", 1).reshape(layers, block, samples)
    (early,) = lax.optimization_barrier((expression,))
    opening = jnp.where(part == 0, early[:, :step], early[:, step:2 * step])
    local, opening = lax.optimization_barrier((local, opening))
    others = jnp.stack(
        [
            lax.dynamic_index_in_dim(local.reshape(layers, block, -1), (layer + 1 + i) % layers, 0, False)
            for i in range(layers - 1)
        ]
    )
    out = gathered(lax.ppermute(others, "layer", inward), "col", 2)

    def take(d, index):
        return lax.dynamic_index_in_dim(d, index, axis=0, keepdims=True)

    def take_out(index):
        return take(out, (index - outer - 1) % layers)

    own_far = gathered(jnp.concatenate([take(own, near), take(own, far)])[None], "row", 0)
    out_far = gathered(jnp.concatenate([take_out(near), take_out(far)])[None], "row", 0)
    far_blocks = jnp.stack([own_far, out_far], axis=1)
    both_far = far_blocks.transpose(2, 0, 3, 1, 4).reshape(2 * rows * block, 2 * samples)

    rest = jnp.concatenate([take(own, layer), take_out(layer), take(own, outer)])
    rest = gathered(rest[None], "row", 0)
    both_here = rest[:, :2].transpose(0, 2, 1, 3).reshape(rows * block, 2 * samples)
    own_outer = rest[:, 2].reshape(rows * block, samples)
    stripe = rows * block

    output = jnp.zeros((block, rows * width), jnp.float32)

    skip = [(half, 0), (half - 1, layers - 1)]

    def finish(output, k, mine, stacked, got):
        if isinstance(got, tuple):
            got_here, got_far, from_inner = got
            final = contract(both_here, stacked) + got_here + got_far + from_inner
        else:
            to_outer = contract(own_outer, mine) + got[stripe:]
            from_inner = lax.ppermute(to_outer, "layer", outward)
            final = contract(both_here, stacked) + got[:stripe] + from_inner
        final = (final * factor).reshape(rows, block, step)
        for shift in range(rows):
            target = (row + shift) % rows
            piece = lax.dynamic_index_in_dim(final, target, axis=0, keepdims=False)
            if shift:
                pairs = [(source, (source + shift) % rows) for source in range(rows)]
                piece = lax.ppermute(piece, "row", pairs)
            source = (row - shift) % rows
            output = lax.dynamic_update_slice_in_dim(output, piece, source * width + k * step, 1)
        return output

    previous = None
    pending = None
    for j in range(chunks // 2):
        first = 2 * j + part
        second = 2 * j + 1 - part
        mine = opening if j == 0 else columns(first)
        if previous is not None:
            mine, _ = lax.optimization_barrier((mine, previous))
        theirs = lax.ppermute(mine, "layer", inward)
        swapped = lax.ppermute(theirs, "parts", swap)
        if j >= 2:
            output, swapped = lax.optimization_barrier((output, swapped))
        for k, mine in [(first, mine), (second, columns(second))]:
            if k is second:
                theirs = swapped
            stacked = jnp.concatenate([mine, theirs], axis=0)
            sent = contract(both_far, stacked)
            if k is first:
                previous = sent
            if j == chunks // 2 - 1:
                got = (
                    lax.ppermute(sent[:stripe], "layer", across),
                    lax.ppermute(sent[stripe:], "layer", skip),
                    lax.ppermute(contract(own_outer, mine), "layer", outward),
                )
            else:
                got = lax.ppermute(sent, "layer", across)
            if pending is not None:
                if k is first:
                    got_before, _, swapped = lax.optimization_barrier((pending[3], sent, swapped))
                else:
                    got_before, _ = lax.optimization_barrier((pending[3], sent))
                output = finish(output, pending[0], pending[1], pending[2], got_before)
            pending = (k, mine, stacked, got)
    output = finish(output, pending[0], pending[1], pending[2], pending[3])
    return output


def solution(mesh):
    return jax.shard_map(
        on_device,
        mesh=mesh,
        in_specs=(P(("layer", "col"), ("parts", "row")), P("layer", ("col", "row"))),
        out_specs=P(("parts", "row", "layer"), "col"),
        check_vma=False,
    )
```

```python
import math

import jax
import jax.numpy as jnp
from jax import lax
from jax.sharding import PartitionSpec as P


def contract(left, right):
    return lax.dot_general(left, right, (((1,), (0,)), ((), ())), preferred_element_type=jnp.float32)


def gathered(value, axis, dim):
    if lax.axis_size(axis) != 2:
        return lax.all_gather(value, axis, axis=dim, tiled=True)
    other = lax.ppermute(value, axis, [(0, 1), (1, 0)])
    first = lax.axis_index(axis) == 0
    return jnp.where(
        first, jnp.concatenate([value, other], dim), jnp.concatenate([other, value], dim)
    )


def on_device(dosages, expression):
    layers = lax.axis_size("layer")
    rows = lax.axis_size("row")
    layer = lax.axis_index("layer")
    row = lax.axis_index("row")
    part = lax.axis_index("parts")
    factor = 1.0 / math.sqrt(dosages.shape[0] * lax.axis_size("col") * layers)

    samples, width = expression.shape
    block = dosages.shape[1] // layers
    half = layers // 2

    inward = [(0, 1), (layers - 1, layers - 2)]
    across = [(half - 1, half), (half, half - 1)]
    outward = [(1, 0), (layers - 2, layers - 1)]
    swap = [(0, 1), (1, 0)]

    is_left = layer < half
    outer = jnp.where(is_left, 0, layers - 1)
    near = layers - 1 - layer
    far = layers - 1 - outer

    chunks = 2 * max(1, min(4, width // 1024))
    step = width // chunks

    def columns(k):
        return lax.dynamic_slice_in_dim(expression, k * step, step, 1)

    local = dosages.T
    own = gathered(local, "col", 1).reshape(layers, block, samples)
    (early,) = lax.optimization_barrier((expression,))
    opening = jnp.where(part == 0, early[:, :step], early[:, step:2 * step])
    local, opening = lax.optimization_barrier((local, opening))
    receiver = jnp.where(layer < half, layer + 1, layer - 1)
    blocks = local.reshape(layers, block, -1)

    def block_of(index):
        return lax.dynamic_index_in_dim(blocks, index, 0, True)

    pair = jnp.concatenate([block_of(layers - 1 - receiver), block_of(layers - 1 - layer)])
    out_pair = gathered(lax.ppermute(pair, "layer", inward), "col", 2)
    out_here = gathered(lax.ppermute(block_of(receiver), "layer", inward), "col", 2)

    def take(d, index):
        return lax.dynamic_index_in_dim(d, index, axis=0, keepdims=True)

    own_far = gathered(jnp.concatenate([take(own, near), take(own, far)])[None], "row", 0)
    out_far = gathered(out_pair[None], "row", 0)
    far_blocks = jnp.stack([own_far, out_far], axis=1)
    both_far = far_blocks.transpose(2, 0, 3, 1, 4).reshape(2 * rows * block, 2 * samples)

    rest = jnp.concatenate([take(own, layer), out_here, take(own, outer)])
    rest = gathered(rest[None], "row", 0)
    both_here = rest[:, :2].transpose(0, 2, 1, 3).reshape(rows * block, 2 * samples)
    own_outer = rest[:, 2].reshape(rows * block, samples)
    stripe = rows * block

    output = jnp.zeros((block, rows * width), jnp.float32)

    skip = [(half, 0), (half - 1, layers - 1)]

    def finish(output, k, mine, stacked, got):
        if isinstance(got, tuple):
            got_here, got_far, from_inner = got
            final = contract(both_here, stacked) + got_here + got_far + from_inner
        else:
            to_outer = contract(own_outer, mine) + got[stripe:]
            from_inner = lax.ppermute(to_outer, "layer", outward)
            final = contract(both_here, stacked) + got[:stripe] + from_inner
        final = (final * factor).reshape(rows, block, step)
        for shift in range(rows):
            target = (row + shift) % rows
            piece = lax.dynamic_index_in_dim(final, target, axis=0, keepdims=False)
            if shift:
                pairs = [(source, (source + shift) % rows) for source in range(rows)]
                piece = lax.ppermute(piece, "row", pairs)
            source = (row - shift) % rows
            output = lax.dynamic_update_slice_in_dim(output, piece, source * width + k * step, 1)
        return output

    previous = None
    pending = None
    for j in range(chunks // 2):
        first = 2 * j + part
        second = 2 * j + 1 - part
        mine = opening if j == 0 else columns(first)
        if previous is not None:
            mine, _ = lax.optimization_barrier((mine, previous))
        theirs = lax.ppermute(mine, "layer", inward)
        swapped = lax.ppermute(theirs, "parts", swap)
        for k, mine in [(first, mine), (second, columns(second))]:
            if k is second:
                theirs = swapped
            stacked = jnp.concatenate([mine, theirs], axis=0)
            sent = contract(both_far, stacked)
            if k is first:
                previous = sent
            if j == chunks // 2 - 1:
                got = (
                    lax.ppermute(sent[:stripe], "layer", across),
                    lax.ppermute(sent[stripe:], "layer", skip),
                    lax.ppermute(contract(own_outer, mine), "layer", outward),
                )
            else:
                got = lax.ppermute(sent, "layer", across)
            if pending is not None:
                if k is first:
                    got_before, _, swapped = lax.optimization_barrier((pending[3], sent, swapped))
                else:
                    got_before, _ = lax.optimization_barrier((pending[3], sent))
                output = finish(output, pending[0], pending[1], pending[2], got_before)
            pending = (k, mine, stacked, got)
    output = finish(output, pending[0], pending[1], pending[2], pending[3])
    return output


def solution(mesh):
    return jax.shard_map(
        on_device,
        mesh=mesh,
        in_specs=(P(("layer", "col"), ("parts", "row")), P("layer", ("col", "row"))),
        out_specs=P(("parts", "row", "layer"), "col"),
        check_vma=False,
    )
```

```python
import math

import jax
import jax.numpy as jnp
from jax import lax
from jax.sharding import PartitionSpec as P


def contract(left, right):
    return lax.dot_general(left, right, (((1,), (0,)), ((), ())), preferred_element_type=jnp.float32)


def gathered(value, axis, dim):
    if lax.axis_size(axis) != 2:
        return lax.all_gather(value, axis, axis=dim, tiled=True)
    other = lax.ppermute(value, axis, [(0, 1), (1, 0)])
    first = lax.axis_index(axis) == 0
    return jnp.where(
        first, jnp.concatenate([value, other], dim), jnp.concatenate([other, value], dim)
    )


def on_device(dosages, expression):
    layers = lax.axis_size("layer")
    rows = lax.axis_size("row")
    layer = lax.axis_index("layer")
    row = lax.axis_index("row")
    part = lax.axis_index("parts")
    factor = 1.0 / math.sqrt(dosages.shape[0] * lax.axis_size("col") * layers)

    samples, width = expression.shape
    block = dosages.shape[1] // layers
    half = layers // 2

    inward = [(0, 1), (layers - 1, layers - 2)]
    across = [(half - 1, half), (half, half - 1)]
    outward = [(1, 0), (layers - 2, layers - 1)]
    swap = [(0, 1), (1, 0)]

    is_left = layer < half
    outer = jnp.where(is_left, 0, layers - 1)
    near = layers - 1 - layer
    far = layers - 1 - outer

    chunks = 2 * max(1, min(4, width // 1024))
    step = width // chunks

    def columns(k):
        return lax.dynamic_slice_in_dim(expression, k * step, step, 1)

    local = dosages.T
    own = gathered(local, "col", 1).reshape(layers, block, samples)
    (early,) = lax.optimization_barrier((expression,))
    opening = jnp.where(part == 0, early[:, :step], early[:, step:2 * step])
    others = jnp.stack(
        [
            lax.dynamic_index_in_dim(local.reshape(layers, block, -1), (layer + 1 + i) % layers, 0, False)
            for i in range(layers - 1)
        ]
    )
    out = gathered(lax.ppermute(others, "layer", inward), "col", 2)

    def take(d, index):
        return lax.dynamic_index_in_dim(d, index, axis=0, keepdims=True)

    def take_out(index):
        return take(out, (index - outer - 1) % layers)

    own_far = gathered(jnp.concatenate([take(own, near), take(own, far)])[None], "row", 0)
    out_far = gathered(jnp.concatenate([take_out(near), take_out(far)])[None], "row", 0)
    far_blocks = jnp.stack([own_far, out_far], axis=1)
    both_far = far_blocks.transpose(2, 0, 3, 1, 4).reshape(2 * rows * block, 2 * samples)

    rest = jnp.concatenate([take(own, layer), take_out(layer), take(own, outer)])
    rest = gathered(rest[None], "row", 0)
    both_here = rest[:, :2].transpose(0, 2, 1, 3).reshape(rows * block, 2 * samples)
    own_outer = rest[:, 2].reshape(rows * block, samples)
    stripe = rows * block

    output = jnp.zeros((block, rows * width), jnp.float32)

    skip = [(half, 0), (half - 1, layers - 1)]

    def finish(output, k, mine, stacked, got):
        if isinstance(got, tuple):
            got_here, got_far, from_inner = got
            final = contract(both_here, stacked) + got_here + got_far + from_inner
        else:
            to_outer = contract(own_outer, mine) + got[stripe:]
            from_inner = lax.ppermute(to_outer, "layer", outward)
            final = contract(both_here, stacked) + got[:stripe] + from_inner
        final = (final * factor).reshape(rows, block, step)
        for shift in range(rows):
            target = (row + shift) % rows
            piece = lax.dynamic_index_in_dim(final, target, axis=0, keepdims=False)
            if shift:
                pairs = [(source, (source + shift) % rows) for source in range(rows)]
                piece = lax.ppermute(piece, "row", pairs)
            source = (row - shift) % rows
            output = lax.dynamic_update_slice_in_dim(output, piece, source * width + k * step, 1)
        return output

    previous = None
    pending = None
    for j in range(chunks // 2):
        first = 2 * j + part
        second = 2 * j + 1 - part
        mine = opening if j == 0 else columns(first)
        if previous is not None:
            mine, _ = lax.optimization_barrier((mine, previous))
        theirs = lax.ppermute(mine, "layer", inward)
        swapped = lax.ppermute(theirs, "parts", swap)
        for k, mine in [(first, mine), (second, columns(second))]:
            if k is second:
                theirs = swapped
            stacked = jnp.concatenate([mine, theirs], axis=0)
            sent = contract(both_far, stacked)
            if k is first:
                previous = sent
            if j == chunks // 2 - 1:
                got = (
                    lax.ppermute(sent[:stripe], "layer", across),
                    lax.ppermute(sent[stripe:], "layer", skip),
                    lax.ppermute(contract(own_outer, mine), "layer", outward),
                )
            else:
                got = lax.ppermute(sent, "layer", across)
            if pending is not None:
                if k is first:
                    got_before, _, swapped = lax.optimization_barrier((pending[3], sent, swapped))
                else:
                    got_before, _ = lax.optimization_barrier((pending[3], sent))
                output = finish(output, pending[0], pending[1], pending[2], got_before)
            pending = (k, mine, stacked, got)
    output = finish(output, pending[0], pending[1], pending[2], pending[3])
    return output


def solution(mesh):
    return jax.shard_map(
        on_device,
        mesh=mesh,
        in_specs=(P(("layer", "col"), ("parts", "row")), P("layer", ("col", "row"))),
        out_specs=P(("parts", "row", "layer"), "col"),
        check_vma=False,
    )
```
